512 devices in a mesh: dp: 16 (over x, y), agent: 32 (over z, core).
Axes of the slice: x: 4, y: 4, z: 16, core: 2. Of those that a mesh axis runs over, the one named last changes fastest.
Arguments:
- activations: bfloat16 [65536, 4096], P(('dp', 'agent')), may hold values from -6 to 6
- row_agent_index: int32 [65536, 1], P(('dp', 'agent')), may hold values from 0 to 31; in each aligned block of 128 rows (0 to 127, 128 to 255, ...) at most 8 rows name the same one
- output_gradient: bfloat16 [65536, 1024], P(('dp', 'agent')), may hold values from -6 to 6
- frozen_value_weight: bfloat16 [4096, 1024], P(('dp', 'agent')), may hold values from -0.09375 to 0.09375
- adapter_down_weight: bfloat16 [32, 64, 4096], P('agent'), may hold values from -0.09375 to 0.09375
- adapter_up_weight: bfloat16 [32, 64, 1024], P('agent'), may hold values from -0.1875 to 0.1875
Outputs:
- value_output: bfloat16 [65536, 1024], P(('dp', 'agent'))
- input_grad: bfloat16 [65536, 4096], P(('dp', 'agent'))
- down_grad: float32 [32, 64, 4096], P('agent')
- up_grad: float32 [32, 64, 1024], P('agent')
The draws below stay inside these ranges and needn't reach their ends.
Inputs may be any that keep to these rules, and one draw needn't show every extreme that they name: `row_agent_index`: within the rows of one device no agent is named more than 8 times, a bound that some block reaches in some devices' rows.
All inputs are finite; a program needn't handle non-finite values.
Results may differ from the reference program's by a relative error of at most 0.0034.
Values may be sent and summed in bfloat16 or wider, within the bound.
No kernel may reach another device: no remote copies, remote signals or barrier semaphores. Data moves between devices by JAX's collectives and lax.ppermute only.
A program may use at most 64 MiB of HBM per device.

```python
import math
import jax
import jax.numpy as jnp
import numpy as np
from jax import lax

MODEL_DIM = 4096
VALUE_HEADS_DIM = 1024
ADAPTER_RANK = 64
TOK_DEV = 128
AGENT_COUNT = 32
CAP = 8
TOKEN_TOTAL = 65536
AGENT_ROWS = 2048
N_DP = 16
N_AGENT = 32


def shard_levels(stream_key, dims, pieces, low, largest):
    loudness = 1.0
    for axis_at, parts in pieces:
        draws = jax.random.uniform(jax.random.fold_in(jax.random.fold_in(stream_key, 6), axis_at), (parts,), jnp.float32, low / len(pieces), largest / len(pieces))
        loudness = loudness * jnp.repeat(jnp.exp(draws), dims[axis_at] // parts).reshape((-1,) + (1,) * (len(dims) - 1 - axis_at))
    return loudness


def deal_out(rng, own, number, rows, count, top, bound, lean):
    ranking = jax.random.permutation(rng, count)
    crowded, usual = load_shares(count, rows * top, bound, lean, True), load_shares(count, rows * top, bound, lean, False)
    places = jnp.arange(count)

    def named(tallies, offset_by):
        used = int((tallies > 0).sum())
        fixed = max(1, used // 4)
        shifted = fixed + (places - fixed + offset_by * (used - fixed)) % max(1, count - fixed)
        return jnp.zeros((count,), jnp.int32).at[ranking[jnp.where(places < fixed, places, shifted)]].set(jnp.asarray(tallies, jnp.int32))

    tallies = jnp.where(number % 4 == 0, named(crowded, number // 4), named(usual, number - number // 4 - 1))
    mixed = jax.random.permutation(jax.random.fold_in(own, 3), count)
    donor, taker = mixed[0:count // 2 * 2:2], mixed[1:count // 2 * 2:2]
    margin = jnp.minimum(tallies[donor] - 1, bound - tallies[taker]) // 2
    margin = jnp.where((donor == ranking[0]) | (taker == ranking[0]) | (tallies[taker] == 0), 0, jnp.maximum(margin, 0))
    shifted = jax.random.randint(jax.random.fold_in(own, 4), (count // 2,), 0, 1 << 20) % (margin + 1)
    tallies = tallies.at[donor].add(-shifted).at[taker].add(shifted)
    items = jnp.searchsorted(jnp.cumsum(tallies), jnp.arange(rows * top), side="right").astype(jnp.int32)
    listing = items.reshape(top, rows).T
    listing = listing[jax.random.permutation(jax.random.fold_in(own, 1), rows)]
    offset_by = jax.random.randint(jax.random.fold_in(own, 2), (rows, 1), 0, top)
    return jnp.take_along_axis(listing, (jnp.arange(top)[None, :] + offset_by) % top, axis=1)


def load_shares(amount, total, limit, lean, full):
    weights = [(1 << 20) // math.isqrt(grade ** lean) + 1 for grade in range(1, amount + 1)]
    largest = limit if full else min(limit, max(-(-total // amount), total * weights[0] // sum(weights)))
    least = 1 if total - largest >= amount - 1 else 0
    counts, spare = [largest] + [least] * (amount - 1), total - largest - least * (amount - 1)
    while spare > 0:
        movable = [i for i in range(1, amount) if counts[i] < largest] or [i for i in range(1, amount) if counts[i] < limit]
        whole, left = sum([weights[i] for i in movable]), spare
        for i in movable:
            extra = min(limit - counts[i], max(1, left * weights[i] // whole), spare)
            counts[i] = counts[i] + extra
            spare = spare - extra
    return np.array(counts)


def gaussian(rng, dims, scale, bound, shards=(), kind=jnp.bfloat16):
    entries = jax.random.normal(rng, dims, jnp.float32) * scale
    if len(shards) > 0:
        entries = shard_levels(rng, dims, shards, -0.22, 0.18) * entries
    return jnp.clip(entries, min=-bound, max=bound).astype(kind)


def setup_inputs(seed: int = 0) -> dict:
    seeds = jax.random.split(jax.random.key(seed), 7)
    activations = gaussian(seeds[0], (TOKEN_TOTAL, MODEL_DIM), 1.0, 6.0, ((0, 512),))
    row_agent_index_keys = jax.random.split(jax.random.fold_in(seeds[1], 1), TOKEN_TOTAL // TOK_DEV)
    row_agent_index_turns = jax.random.permutation(jax.random.fold_in(seeds[1], 3), TOKEN_TOTAL // TOK_DEV)
    row_agent_index = jax.vmap(lambda own, number: deal_out(jax.random.fold_in(seeds[1], 2), own, number, TOK_DEV, AGENT_COUNT, 1, CAP, 2))(row_agent_index_keys, row_agent_index_turns).reshape((TOKEN_TOTAL, 1))
    output_gradient = gaussian(seeds[2], (TOKEN_TOTAL, VALUE_HEADS_DIM), 1.0, 6.0, ((0, 512),))
    frozen_value_weight = gaussian(seeds[3], (MODEL_DIM, VALUE_HEADS_DIM), MODEL_DIM ** -0.5, 0.09375, ((0, 512),))
    adapter_down_weight = gaussian(seeds[4], (AGENT_COUNT, ADAPTER_RANK, MODEL_DIM), MODEL_DIM ** -0.5, 0.09375, ((0, 32),))
    adapter_up_weight = gaussian(seeds[5], (AGENT_COUNT, ADAPTER_RANK, VALUE_HEADS_DIM), VALUE_HEADS_DIM ** -0.5, 0.1875, ((0, 32),))
    return dict(activations=activations, row_agent_index=row_agent_index, output_gradient=output_gradient, frozen_value_weight=frozen_value_weight, adapter_down_weight=adapter_down_weight, adapter_up_weight=adapter_up_weight)


ADAPTER_SCALE = 2.0

def reference(activations, row_agent_index, output_gradient, frozen_value_weight, adapter_down_weight, adapter_up_weight):
    frozen_projection = jnp.dot(activations, frozen_value_weight, preferred_element_type=jnp.float32)
    base_back = lax.dot_general(output_gradient, frozen_value_weight, (((1,), (1,)), ((), ())), preferred_element_type=jnp.float32)
    owner_ids = row_agent_index[:, 0]
    most_rows = CAP * N_DP * N_AGENT
    padded_x = jnp.concatenate([activations, jnp.zeros((1, MODEL_DIM), activations.dtype)], axis=0)
    padded_g = jnp.concatenate([output_gradient, jnp.zeros((1, VALUE_HEADS_DIM), output_gradient.dtype)], axis=0)
    scaled_gradient = 1.0 / math.sqrt(AGENT_ROWS)
    highest = lax.Precision.HIGHEST

    def per_agent(totals, owner_index):
        raised_all_rows, spread_all = totals
        positions = jnp.nonzero(owner_ids == owner_index, size=most_rows, fill_value=TOKEN_TOTAL)[0].astype(jnp.int32)
        rows_x = padded_x[positions]
        row_gradients = padded_g[positions]
        down_weight = adapter_down_weight[owner_index]
        up_weight = adapter_up_weight[owner_index]
        down_wide = down_weight.astype(jnp.float32)
        up_wide = up_weight.astype(jnp.float32)
        rank_reduced = lax.dot_general(rows_x, down_weight, (((1,), (1,)), ((), ())), preferred_element_type=jnp.float32)
        lifted = jnp.dot(rank_reduced, up_wide, precision=highest, preferred_element_type=jnp.float32).astype(jnp.bfloat16)
        collected_rows = ADAPTER_SCALE * lax.dot_general(row_gradients, up_weight, (((1,), (1,)), ((), ())), preferred_element_type=jnp.float32)
        spread = jnp.dot(collected_rows, down_wide, precision=highest, preferred_element_type=jnp.float32).astype(jnp.bfloat16)
        grad_down = lax.dot_general(collected_rows, rows_x.astype(jnp.float32), (((0,), (0,)), ((), ())), precision=highest, preferred_element_type=jnp.float32) * scaled_gradient
        up_weight_gradient = ADAPTER_SCALE * lax.dot_general(rank_reduced, row_gradients.astype(jnp.float32), (((0,), (0,)), ((), ())), precision=highest, preferred_element_type=jnp.float32) * scaled_gradient
        raised_all_rows = raised_all_rows.at[positions].set(lifted)
        spread_all = spread_all.at[positions].set(spread)
        return ((raised_all_rows, spread_all), (grad_down, up_weight_gradient))
    start_state = (jnp.zeros((TOKEN_TOTAL + 1, VALUE_HEADS_DIM), jnp.bfloat16), jnp.zeros((TOKEN_TOTAL + 1, MODEL_DIM), jnp.bfloat16))
    (raised_all_rows, spread_all), (down_grad, up_grad) = lax.scan(per_agent, start_state, jnp.arange(AGENT_COUNT, dtype=jnp.int32))
    value_output = (frozen_projection + ADAPTER_SCALE * raised_all_rows[:TOKEN_TOTAL].astype(jnp.float32)).astype(jnp.bfloat16)
    input_grad = (base_back + spread_all[:TOKEN_TOTAL].astype(jnp.float32)).astype(jnp.bfloat16)
    return (value_output, input_grad, down_grad, up_grad)
```

```python
import math

import jax
import jax.numpy as jnp
from jax import lax
from jax.sharding import PartitionSpec as P

ADAPTER_SCALE = 2.0


def per_device(
    activations,
    row_agent_index,
    output_gradient,
    frozen_value_weight,
    adapter_down_weight,
    adapter_up_weight,
):
    groups = lax.axis_size("agent")
    tok_rows = activations.shape[0]
    model_width = activations.shape[1]
    value_width = output_gradient.shape[1]
    capacity = 2 * tok_rows // groups
    slot_count = groups * capacity
    scaled_gradient = 1.0 / math.sqrt(tok_rows * lax.axis_size("dp"))
    highest = lax.Precision.HIGHEST
    owner_ids = row_agent_index[:, 0]
    onehot = (owner_ids[:, None] == jnp.arange(groups, dtype=jnp.int32)[None, :]).astype(
        jnp.bfloat16
    )
    earlier = (jnp.arange(tok_rows)[None, :] < jnp.arange(tok_rows)[:, None]).astype(jnp.bfloat16)
    before = jnp.dot(earlier, onehot, preferred_element_type=jnp.float32)
    slot_rank = jnp.sum(before * onehot.astype(jnp.float32), axis=1).astype(jnp.int32)
    target = owner_ids * capacity + slot_rank
    packing = (jnp.arange(slot_count, dtype=jnp.int32)[:, None] == target[None, :]).astype(
        jnp.bfloat16
    )
    plane_weight = lax.all_gather(frozen_value_weight, "agent", axis=0, tiled=True)
    whole_weight = lax.all_gather(plane_weight, "dp", axis=0, tiled=True)
    value_projected = jnp.dot(activations, whole_weight, preferred_element_type=jnp.float32)
    backward = lax.dot_general(
        output_gradient, whole_weight, (((1,), (1,)), ((), ())), preferred_element_type=jnp.float32
    )
    value_projected, backward = (value_projected, backward)
    both = jnp.concatenate([activations, output_gradient], axis=1)
    send = jnp.dot(packing, both, preferred_element_type=jnp.float32).astype(jnp.bfloat16)
    recv = lax.all_to_all(
        send.reshape(groups, capacity, model_width + value_width),
        "agent",
        split_axis=0,
        concat_axis=0,
        tiled=True,
    ).reshape(slot_count, model_width + value_width)
    rows_x = recv[:, :model_width]
    row_gradients = recv[:, model_width:]
    down_weight = adapter_down_weight[0]
    up_weight = adapter_up_weight[0]
    down_wide = down_weight.astype(jnp.float32)
    up_wide = up_weight.astype(jnp.float32)
    rank_reduced = lax.dot_general(
        rows_x, down_weight, (((1,), (1,)), ((), ())), preferred_element_type=jnp.float32
    )
    lifted = jnp.dot(
        rank_reduced, up_wide, precision=highest, preferred_element_type=jnp.float32
    ).astype(jnp.bfloat16)
    collected_rows = ADAPTER_SCALE * lax.dot_general(
        row_gradients, up_weight, (((1,), (1,)), ((), ())), preferred_element_type=jnp.float32
    )
    spread = jnp.dot(
        collected_rows, down_wide, precision=highest, preferred_element_type=jnp.float32
    ).astype(jnp.bfloat16)
    grad_down = (
        lax.dot_general(
            collected_rows,
            rows_x.astype(jnp.float32),
            (((0,), (0,)), ((), ())),
            precision=highest,
            preferred_element_type=jnp.float32,
        )
        * scaled_gradient
    )
    up_weight_gradient = (
        ADAPTER_SCALE
        * lax.dot_general(
            rank_reduced,
            row_gradients.astype(jnp.float32),
            (((0,), (0,)), ((), ())),
            precision=highest,
            preferred_element_type=jnp.float32,
        )
        * scaled_gradient
    )
    back = lax.all_to_all(
        jnp.concatenate([spread, lifted], axis=1).reshape(groups, capacity, model_width + value_width),
        "agent",
        split_axis=0,
        concat_axis=0,
        tiled=True,
    ).reshape(slot_count, model_width + value_width)
    grad_down, up_weight_gradient = lax.psum((grad_down, up_weight_gradient), "dp")
    raised_rows = lax.dot_general(
        packing,
        back[:, model_width:],
        (((0,), (0,)), ((), ())),
        preferred_element_type=jnp.float32,
    )
    spread_rows = lax.dot_general(
        packing,
        back[:, :model_width],
        (((0,), (0,)), ((), ())),
        preferred_element_type=jnp.float32,
    )
    raised_rows, spread_rows, down_grad, up_grad = (
        raised_rows,
        spread_rows,
        grad_down[None],
        up_weight_gradient[None],
    )
    value_output = (value_projected + ADAPTER_SCALE * raised_rows).astype(jnp.bfloat16)
    input_grad = (backward + spread_rows).astype(jnp.bfloat16)
    return (value_output, input_grad, down_grad, up_grad)


def solution(mesh):
    return jax.shard_map(
        per_device,
        mesh=mesh,
        in_specs=(
            P(("dp", "agent"), None),
            P(("dp", "agent"), None),
            P(("dp", "agent"), None),
            P(("dp", "agent"), None),
            P("agent", None, None),
            P("agent", None, None),
        ),
        out_specs=(
            P(("dp", "agent"), None),
            P(("dp", "agent"), None),
            P("agent", None, None),
            P("agent", None, None),
        ),
        check_vma=False,
    )
```

```python
import math

import jax
import jax.numpy as jnp
from jax import lax
from jax.sharding import PartitionSpec as P

ADAPTER_SCALE = 2.0


def _dp_sum(grad_down, grad_up):
    parts = lax.axis_size("dp")
    flat = jnp.concatenate([grad_down.reshape(-1), grad_up.reshape(-1)])
    chunks = flat.reshape(parts, flat.shape[0] // parts)
    mine = jnp.sum(
        lax.all_to_all(chunks, "dp", split_axis=0, concat_axis=0, tiled=True), axis=0
    )
    every = lax.all_to_all(
        jnp.broadcast_to(mine[None], chunks.shape), "dp", split_axis=0, concat_axis=0, tiled=True
    ).reshape(-1)
    split = grad_down.size
    return every[:split].reshape(grad_down.shape), every[split:].reshape(grad_up.shape)


def per_device(
    activations,
    row_agent_index,
    output_gradient,
    frozen_value_weight,
    adapter_down_weight,
    adapter_up_weight,
):
    groups = lax.axis_size("agent")
    tok_rows = activations.shape[0]
    model_width = activations.shape[1]
    value_width = output_gradient.shape[1]
    capacity = 2 * tok_rows // groups
    slot_count = groups * capacity
    scaled_gradient = 1.0 / math.sqrt(tok_rows * lax.axis_size("dp"))
    highest = lax.Precision.HIGHEST
    owner_ids = row_agent_index[:, 0]
    onehot = (owner_ids[:, None] == jnp.arange(groups, dtype=jnp.int32)[None, :]).astype(
        jnp.bfloat16
    )
    earlier = (jnp.arange(tok_rows)[None, :] < jnp.arange(tok_rows)[:, None]).astype(jnp.bfloat16)
    before = jnp.dot(earlier, onehot, preferred_element_type=jnp.float32)
    slot_rank = jnp.sum(before * onehot.astype(jnp.float32), axis=1).astype(jnp.int32)
    target = owner_ids * capacity + slot_rank
    packing = (jnp.arange(slot_count, dtype=jnp.int32)[:, None] == target[None, :]).astype(
        jnp.bfloat16
    )
    plane_weight = lax.all_gather(frozen_value_weight, "agent", axis=0, tiled=True)
    both = jnp.concatenate([activations, output_gradient], axis=1)
    send = jnp.dot(packing, both, preferred_element_type=jnp.float32).astype(jnp.bfloat16)
    plane_weight, send = lax.optimization_barrier((plane_weight, send))
    whole_weight = lax.all_gather(plane_weight, "dp", axis=0, tiled=True)
    value_projected = jnp.dot(activations, whole_weight, preferred_element_type=jnp.float32)
    backward = lax.dot_general(
        output_gradient, whole_weight, (((1,), (1,)), ((), ())), preferred_element_type=jnp.float32
    )
    recv = lax.all_to_all(
        send.reshape(groups, capacity, model_width + value_width),
        "agent",
        split_axis=0,
        concat_axis=0,
        tiled=True,
    ).reshape(slot_count, model_width + value_width)
    rows_x = recv[:, :model_width]
    row_gradients = recv[:, model_width:]
    down_weight = adapter_down_weight[0]
    up_weight = adapter_up_weight[0]
    down_wide = down_weight.astype(jnp.float32)
    up_wide = up_weight.astype(jnp.float32)
    rank_reduced = lax.dot_general(
        rows_x, down_weight, (((1,), (1,)), ((), ())), preferred_element_type=jnp.float32
    )
    lifted = jnp.dot(
        rank_reduced, up_wide, precision=highest, preferred_element_type=jnp.float32
    ).astype(jnp.bfloat16)
    collected_rows = ADAPTER_SCALE * lax.dot_general(
        row_gradients, up_weight, (((1,), (1,)), ((), ())), preferred_element_type=jnp.float32
    )
    spread = jnp.dot(
        collected_rows, down_wide, precision=highest, preferred_element_type=jnp.float32
    ).astype(jnp.bfloat16)
    grad_down = (
        lax.dot_general(
            collected_rows,
            rows_x.astype(jnp.float32),
            (((0,), (0,)), ((), ())),
            precision=highest,
            preferred_element_type=jnp.float32,
        )
        * scaled_gradient
    )
    up_weight_gradient = (
        ADAPTER_SCALE
        * lax.dot_general(
            rank_reduced,
            row_gradients.astype(jnp.float32),
            (((0,), (0,)), ((), ())),
            precision=highest,
            preferred_element_type=jnp.float32,
        )
        * scaled_gradient
    )
    back = lax.all_to_all(
        jnp.concatenate([spread, lifted], axis=1).reshape(groups, capacity, model_width + value_width),
        "agent",
        split_axis=0,
        concat_axis=0,
        tiled=True,
    ).reshape(slot_count, model_width + value_width)
    grad_down, up_weight_gradient = _dp_sum(grad_down, up_weight_gradient)
    raised_rows = lax.dot_general(
        packing,
        back[:, model_width:],
        (((0,), (0,)), ((), ())),
        preferred_element_type=jnp.float32,
    )
    spread_rows = lax.dot_general(
        packing,
        back[:, :model_width],
        (((0,), (0,)), ((), ())),
        preferred_element_type=jnp.float32,
    )
    raised_rows, spread_rows, down_grad, up_grad = (
        raised_rows,
        spread_rows,
        grad_down[None],
        up_weight_gradient[None],
    )
    value_output = (value_projected + ADAPTER_SCALE * raised_rows).astype(jnp.bfloat16)
    input_grad = (backward + spread_rows).astype(jnp.bfloat16)
    return (value_output, input_grad, down_grad, up_grad)


def solution(mesh):
    return jax.shard_map(
        per_device,
        mesh=mesh,
        in_specs=(
            P(("dp", "agent"), None),
            P(("dp", "agent"), None),
            P(("dp", "agent"), None),
            P(("dp", "agent"), None),
            P("agent", None, None),
            P("agent", None, None),
        ),
        out_specs=(
            P(("dp", "agent"), None),
            P(("dp", "agent"), None),
            P("agent", None, None),
            P("agent", None, None),
        ),
        check_vma=False,
    )
```

```python
import math

import jax
import jax.numpy as jnp
from jax import lax
from jax.sharding import PartitionSpec as P

ADAPTER_SCALE = 2.0


def _dp_sum(grad_down, grad_up):
    parts = lax.axis_size("dp")
    flat = jnp.concatenate([grad_down.reshape(-1), grad_up.reshape(-1)])
    chunks = flat.reshape(parts, flat.shape[0] // parts)
    mine = jnp.sum(
        lax.all_to_all(chunks, "dp", split_axis=0, concat_axis=0, tiled=True), axis=0
    )
    every = lax.all_to_all(
        jnp.broadcast_to(mine[None], chunks.shape), "dp", split_axis=0, concat_axis=0, tiled=True
    ).reshape(-1)
    split = grad_down.size
    return every[:split].reshape(grad_down.shape), every[split:].reshape(grad_up.shape)


def _gather_adapter(weight):
    parts = lax.axis_size("dp")
    rank = weight.shape[0]
    piece = rank // parts
    mine = lax.dynamic_slice_in_dim(weight, lax.axis_index("dp") * piece, piece, 0)
    plane = lax.all_gather(mine, "agent", axis=0, tiled=False)
    return lax.all_gather(plane, "dp", axis=1, tiled=True)


def per_device(
    activations,
    row_agent_index,
    output_gradient,
    frozen_value_weight,
    adapter_down_weight,
    adapter_up_weight,
):
    groups = lax.axis_size("agent")
    tok_rows = activations.shape[0]
    model_width = activations.shape[1]
    value_width = output_gradient.shape[1]
    capacity = 2 * tok_rows // groups
    slot_count = groups * capacity
    scaled_gradient = 1.0 / math.sqrt(tok_rows * lax.axis_size("dp"))
    highest = lax.Precision.HIGHEST
    owner_ids = row_agent_index[:, 0]
    onehot = (owner_ids[:, None] == jnp.arange(groups, dtype=jnp.int32)[None, :]).astype(
        jnp.bfloat16
    )
    earlier = (jnp.arange(tok_rows)[None, :] < jnp.arange(tok_rows)[:, None]).astype(jnp.bfloat16)
    before = jnp.dot(earlier, onehot, preferred_element_type=jnp.float32)
    slot_rank = jnp.sum(before * onehot.astype(jnp.float32), axis=1).astype(jnp.int32)
    target = owner_ids * capacity + slot_rank
    packing = (jnp.arange(slot_count, dtype=jnp.int32)[:, None] == target[None, :]).astype(
        jnp.bfloat16
    )
    both = jnp.concatenate([activations, output_gradient], axis=1)
    send = jnp.dot(packing, both, preferred_element_type=jnp.float32).astype(jnp.bfloat16)

    recv = lax.all_to_all(
        send.reshape(groups, capacity, model_width + value_width),
        "agent",
        split_axis=0,
        concat_axis=0,
        tiled=True,
    ).reshape(slot_count, model_width + value_width)

    all_down = _gather_adapter(adapter_down_weight[0])
    all_up = _gather_adapter(adapter_up_weight[0])
    plane_weight = lax.all_gather(frozen_value_weight, "agent", axis=0, tiled=True)
    whole_weight = lax.all_gather(plane_weight, "dp", axis=0, tiled=True)

    slots = send.reshape(groups, capacity, model_width + value_width)
    slot_x = slots[:, :, :model_width]
    slot_g = slots[:, :, model_width:]
    slot_low = jnp.einsum("akd,ard->akr", slot_x, all_down, preferred_element_type=jnp.float32)
    slot_pull = ADAPTER_SCALE * jnp.einsum(
        "akv,arv->akr", slot_g, all_up, preferred_element_type=jnp.float32
    )
    slot_lifted = jnp.einsum(
        "akr,arv->akv",
        slot_low,
        all_up.astype(jnp.float32),
        precision=highest,
        preferred_element_type=jnp.float32,
    ).astype(jnp.bfloat16)
    slot_spread = jnp.einsum(
        "akr,ard->akd",
        slot_pull,
        all_down.astype(jnp.float32),
        precision=highest,
        preferred_element_type=jnp.float32,
    ).astype(jnp.bfloat16)
    raised_rows = lax.dot_general(
        packing,
        slot_lifted.reshape(slot_count, value_width),
        (((0,), (0,)), ((), ())),
        preferred_element_type=jnp.float32,
    )
    spread_rows = lax.dot_general(
        packing,
        slot_spread.reshape(slot_count, model_width),
        (((0,), (0,)), ((), ())),
        preferred_element_type=jnp.float32,
    )
    value_projected = jnp.dot(activations, whole_weight, preferred_element_type=jnp.float32)
    backward = lax.dot_general(
        output_gradient, whole_weight, (((1,), (1,)), ((), ())), preferred_element_type=jnp.float32
    )
    value_output = (value_projected + ADAPTER_SCALE * raised_rows).astype(jnp.bfloat16)
    input_grad = (backward + spread_rows).astype(jnp.bfloat16)

    rows_x = recv[:, :model_width]
    row_gradients = recv[:, model_width:]
    down_weight = adapter_down_weight[0]
    up_weight = adapter_up_weight[0]
    rank_reduced = lax.dot_general(
        rows_x, down_weight, (((1,), (1,)), ((), ())), preferred_element_type=jnp.float32
    )
    collected_rows = ADAPTER_SCALE * lax.dot_general(
        row_gradients, up_weight, (((1,), (1,)), ((), ())), preferred_element_type=jnp.float32
    )
    grad_down = (
        lax.dot_general(
            collected_rows,
            rows_x.astype(jnp.float32),
            (((0,), (0,)), ((), ())),
            precision=highest,
            preferred_element_type=jnp.float32,
        )
        * scaled_gradient
    )
    up_weight_gradient = (
        ADAPTER_SCALE
        * lax.dot_general(
            rank_reduced,
            row_gradients.astype(jnp.float32),
            (((0,), (0,)), ((), ())),
            precision=highest,
            preferred_element_type=jnp.float32,
        )
        * scaled_gradient
    )
    grad_down, up_weight_gradient = _dp_sum(grad_down, up_weight_gradient)
    return (value_output, input_grad, grad_down[None], up_weight_gradient[None])


def solution(mesh):
    return jax.shard_map(
        per_device,
        mesh=mesh,
        in_specs=(
            P(("dp", "agent"), None),
            P(("dp", "agent"), None),
            P(("dp", "agent"), None),
            P(("dp", "agent"), None),
            P("agent", None, None),
            P("agent", None, None),
        ),
        out_specs=(
            P(("dp", "agent"), None),
            P(("dp", "agent"), None),
            P("agent", None, None),
            P("agent", None, None),
        ),
        check_vma=False,
    )
```

```python
import math

import jax
import jax.numpy as jnp
from jax import lax
from jax.sharding import PartitionSpec as P

ADAPTER_SCALE = 2.0


def _dp_sum(grad_down, grad_up):
    parts = lax.axis_size("dp")
    flat = jnp.concatenate([grad_down.reshape(-1), grad_up.reshape(-1)])
    chunks = flat.reshape(parts, flat.shape[0] // parts)
    mine = jnp.sum(
        lax.all_to_all(chunks, "dp", split_axis=0, concat_axis=0, tiled=True), axis=0
    )
    every = lax.all_to_all(
        jnp.broadcast_to(mine[None], chunks.shape), "dp", split_axis=0, concat_axis=0, tiled=True
    ).reshape(-1)
    split = grad_down.size
    return every[:split].reshape(grad_down.shape), every[split:].reshape(grad_up.shape)


def _exact_split(values):
    high = values.astype(jnp.bfloat16)
    rest = values - high.astype(jnp.float32)
    middle = rest.astype(jnp.bfloat16)
    low = (rest - middle.astype(jnp.float32)).astype(jnp.bfloat16)
    return jnp.concatenate([high, middle, low], axis=1)


def _times_weight(small, weight, spec):
    k = small.shape[1]
    out = jnp.einsum(spec, _exact_split(small), weight, preferred_element_type=jnp.float32)
    return out[:, :k] + out[:, k : 2 * k] + out[:, 2 * k :]


def _gather_everything(down, up, weight):
    parts = lax.axis_size("dp")
    agents = lax.axis_size("agent")
    rank, model_width = down.shape
    value_width = up.shape[1]
    piece = rank // parts
    at = lax.axis_index("dp") * piece
    down_piece = lax.dynamic_slice_in_dim(down, at, piece, 0)
    up_piece = lax.dynamic_slice_in_dim(up, at, piece, 0)
    flat = jnp.concatenate([down_piece.reshape(-1), up_piece.reshape(-1), weight.reshape(-1)])
    plane = lax.all_gather(flat, "agent", axis=0, tiled=False)
    cut_d = piece * model_width
    cut_u = cut_d + piece * value_width
    plane_down = plane[:, :cut_d].reshape(agents, piece, model_width)
    plane_up = plane[:, cut_d:cut_u].reshape(agents, piece, value_width)
    plane_w = plane[:, cut_u:].reshape(agents * weight.shape[0], value_width)
    core = lax.axis_index("agent") % 2
    half_d = model_width // 2
    half_v = value_width // 2
    mine_down = lax.dynamic_slice_in_dim(plane_down, core * half_d, half_d, 2)
    mine_up = lax.dynamic_slice_in_dim(plane_up, core * half_v, half_v, 2)
    mine_w = lax.dynamic_slice_in_dim(plane_w, core * half_v, half_v, 1)
    mine_down = lax.all_gather(mine_down, "dp", axis=1, tiled=True)
    mine_up = lax.all_gather(mine_up, "dp", axis=1, tiled=True)
    mine_w = lax.all_gather(mine_w, "dp", axis=0, tiled=True)
    pairs = [(j, j ^ 1) for j in range(agents)]
    other_down, other_up, other_w = lax.ppermute((mine_down, mine_up, mine_w), "agent", pairs)
    return core, (mine_down, mine_up, mine_w), (other_down, other_up, other_w)


def per_device(
    activations,
    row_agent_index,
    output_gradient,
    frozen_value_weight,
    adapter_down_weight,
    adapter_up_weight,
):
    groups = lax.axis_size("agent")
    tok_rows = activations.shape[0]
    model_width = activations.shape[1]
    value_width = output_gradient.shape[1]
    capacity = 2 * tok_rows // groups
    slot_count = groups * capacity
    scaled_gradient = 1.0 / math.sqrt(tok_rows * lax.axis_size("dp"))
    highest = lax.Precision.HIGHEST
    owner_ids = row_agent_index[:, 0]
    onehot = (owner_ids[:, None] == jnp.arange(groups, dtype=jnp.int32)[None, :]).astype(
        jnp.bfloat16
    )
    earlier = (jnp.arange(tok_rows)[None, :] < jnp.arange(tok_rows)[:, None]).astype(jnp.bfloat16)
    before = jnp.dot(earlier, onehot, preferred_element_type=jnp.float32)
    slot_rank = jnp.sum(before * onehot.astype(jnp.float32), axis=1).astype(jnp.int32)
    target = owner_ids * capacity + slot_rank
    packing = (jnp.arange(slot_count, dtype=jnp.int32)[:, None] == target[None, :]).astype(
        jnp.bfloat16
    )
    both = jnp.concatenate([activations, output_gradient], axis=1)
    send = jnp.dot(packing, both, preferred_element_type=jnp.float32).astype(jnp.bfloat16)

    recv = lax.all_to_all(
        send.reshape(groups, capacity, model_width + value_width),
        "agent",
        split_axis=0,
        concat_axis=0,
        tiled=True,
    ).reshape(slot_count, model_width + value_width)

    core, mine, other = _gather_everything(
        adapter_down_weight[0], adapter_up_weight[0], frozen_value_weight
    )
    half_d = model_width // 2
    half_v = value_width // 2

    slots = send.reshape(groups, capacity, model_width + value_width)
    slot_x = slots[:, :, :model_width]
    slot_g = slots[:, :, model_width:]
    x_mine = lax.dynamic_slice_in_dim(slot_x, core * half_d, half_d, 2)
    x_other = lax.dynamic_slice_in_dim(slot_x, (1 - core) * half_d, half_d, 2)
    g_mine = lax.dynamic_slice_in_dim(slot_g, core * half_v, half_v, 2)
    g_other = lax.dynamic_slice_in_dim(slot_g, (1 - core) * half_v, half_v, 2)
    slot_low = jnp.einsum(
        "akd,ard->akr", x_mine, mine[0], preferred_element_type=jnp.float32
    ) + jnp.einsum("akd,ard->akr", x_other, other[0], preferred_element_type=jnp.float32)
    slot_pull = ADAPTER_SCALE * (
        jnp.einsum("akv,arv->akr", g_mine, mine[1], preferred_element_type=jnp.float32)
        + jnp.einsum("akv,arv->akr", g_other, other[1], preferred_element_type=jnp.float32)
    )
    lifted_mine = _times_weight(slot_low, mine[1], "akr,arv->akv").astype(jnp.bfloat16)
    lifted_other = _times_weight(slot_low, other[1], "akr,arv->akv").astype(jnp.bfloat16)
    spread_mine = _times_weight(slot_pull, mine[0], "akr,ard->akd").astype(jnp.bfloat16)
    spread_other = _times_weight(slot_pull, other[0], "akr,ard->akd").astype(jnp.bfloat16)
    first = core == 0
    slot_lifted = jnp.where(
        first,
        jnp.concatenate([lifted_mine, lifted_other], axis=2),
        jnp.concatenate([lifted_other, lifted_mine], axis=2),
    )
    slot_spread = jnp.where(
        first,
        jnp.concatenate([spread_mine, spread_other], axis=2),
        jnp.concatenate([spread_other, spread_mine], axis=2),
    )
    raised_rows = lax.dot_general(
        packing,
        slot_lifted.reshape(slot_count, value_width),
        (((0,), (0,)), ((), ())),
        preferred_element_type=jnp.float32,
    )
    spread_rows = lax.dot_general(
        packing,
        slot_spread.reshape(slot_count, model_width),
        (((0,), (0,)), ((), ())),
        preferred_element_type=jnp.float32,
    )
    proj_mine = jnp.dot(activations, mine[2], preferred_element_type=jnp.float32)
    proj_other = jnp.dot(activations, other[2], preferred_element_type=jnp.float32)
    value_projected = jnp.where(
        first,
        jnp.concatenate([proj_mine, proj_other], axis=1),
        jnp.concatenate([proj_other, proj_mine], axis=1),
    )
    grad_mine = lax.dynamic_slice_in_dim(output_gradient, core * half_v, half_v, 1)
    grad_other = lax.dynamic_slice_in_dim(output_gradient, (1 - core) * half_v, half_v, 1)
    backward = lax.dot_general(
        grad_mine, mine[2], (((1,), (1,)), ((), ())), preferred_element_type=jnp.float32
    ) + lax.dot_general(
        grad_other, other[2], (((1,), (1,)), ((), ())), preferred_element_type=jnp.float32
    )
    value_output = (value_projected + ADAPTER_SCALE * raised_rows).astype(jnp.bfloat16)
    input_grad = (backward + spread_rows).astype(jnp.bfloat16)

    rows_x = recv[:, :model_width]
    row_gradients = recv[:, model_width:]
    down_weight = adapter_down_weight[0]
    up_weight = adapter_up_weight[0]
    rank_reduced = lax.dot_general(
        rows_x, down_weight, (((1,), (1,)), ((), ())), preferred_element_type=jnp.float32
    )
    collected_rows = ADAPTER_SCALE * lax.dot_general(
        row_gradients, up_weight, (((1,), (1,)), ((), ())), preferred_element_type=jnp.float32
    )
    grad_down = (
        lax.dot_general(
            collected_rows,
            rows_x.astype(jnp.float32),
            (((0,), (0,)), ((), ())),
            precision=highest,
            preferred_element_type=jnp.float32,
        )
        * scaled_gradient
    )
    up_weight_gradient = (
        ADAPTER_SCALE
        * lax.dot_general(
            rank_reduced,
            row_gradients.astype(jnp.float32),
            (((0,), (0,)), ((), ())),
            precision=highest,
            preferred_element_type=jnp.float32,
        )
        * scaled_gradient
    )
    grad_down, up_weight_gradient = _dp_sum(grad_down, up_weight_gradient)
    return (value_output, input_grad, grad_down[None], up_weight_gradient[None])


def solution(mesh):
    return jax.shard_map(
        per_device,
        mesh=mesh,
        in_specs=(
            P(("dp", "agent"), None),
            P(("dp", "agent"), None),
            P(("dp", "agent"), None),
            P(("dp", "agent"), None),
            P("agent", None, None),
            P("agent", None, None),
        ),
        out_specs=(
            P(("dp", "agent"), None),
            P(("dp", "agent"), None),
            P("agent", None, None),
            P("agent", None, None),
        ),
        check_vma=False,
    )
```

```python
import math

import jax
import jax.numpy as jnp
from jax import lax
from jax.sharding import PartitionSpec as P

ADAPTER_SCALE = 2.0


def per_device(
    activations,
    row_agent_index,
    output_gradient,
    frozen_value_weight,
    adapter_down_weight,
    adapter_up_weight,
):
    groups = lax.axis_size("agent")
    tok_rows = activations.shape[0]
    model_width = activations.shape[1]
    value_width = output_gradient.shape[1]
    capacity = 2 * tok_rows // groups
    slot_count = groups * capacity
    scaled_gradient = 1.0 / math.sqrt(tok_rows * lax.axis_size("dp"))
    highest = lax.Precision.HIGHEST
    owner_ids = row_agent_index[:, 0]
    onehot = (owner_ids[:, None] == jnp.arange(groups, dtype=jnp.int32)[None, :]).astype(
        jnp.bfloat16
    )
    earlier = (jnp.arange(tok_rows)[None, :] < jnp.arange(tok_rows)[:, None]).astype(jnp.bfloat16)
    before = jnp.dot(earlier, onehot, preferred_element_type=jnp.float32)
    slot_rank = jnp.sum(before * onehot.astype(jnp.float32), axis=1).astype(jnp.int32)
    target = owner_ids * capacity + slot_rank
    packing = (jnp.arange(slot_count, dtype=jnp.int32)[:, None] == target[None, :]).astype(
        jnp.bfloat16
    )
    whole_weight = lax.all_gather(frozen_value_weight, ("dp", "agent"), axis=0, tiled=True)
    value_projected = jnp.dot(activations, whole_weight, preferred_element_type=jnp.float32)
    backward = lax.dot_general(
        output_gradient, whole_weight, (((1,), (1,)), ((), ())), preferred_element_type=jnp.float32
    )
    value_projected, backward = (value_projected, backward)
    both = jnp.concatenate([activations, output_gradient], axis=1)
    send = jnp.dot(packing, both, preferred_element_type=jnp.float32).astype(jnp.bfloat16)
    recv = lax.all_to_all(
        send.reshape(groups, capacity, model_width + value_width),
        "agent",
        split_axis=0,
        concat_axis=0,
        tiled=True,
    ).reshape(slot_count, model_width + value_width)
    rows_x = recv[:, :model_width]
    row_gradients = recv[:, model_width:]
    down_weight = adapter_down_weight[0]
    up_weight = adapter_up_weight[0]
    down_wide = down_weight.astype(jnp.float32)
    up_wide = up_weight.astype(jnp.float32)
    rank_reduced = lax.dot_general(
        rows_x, down_weight, (((1,), (1,)), ((), ())), preferred_element_type=jnp.float32
    )
    lifted = jnp.dot(
        rank_reduced, up_wide, precision=highest, preferred_element_type=jnp.float32
    ).astype(jnp.bfloat16)
    collected_rows = ADAPTER_SCALE * lax.dot_general(
        row_gradients, up_weight, (((1,), (1,)), ((), ())), preferred_element_type=jnp.float32
    )
    spread = jnp.dot(
        collected_rows, down_wide, precision=highest, preferred_element_type=jnp.float32
    ).astype(jnp.bfloat16)
    grad_down = (
        lax.dot_general(
            collected_rows,
            rows_x.astype(jnp.float32),
            (((0,), (0,)), ((), ())),
            precision=highest,
            preferred_element_type=jnp.float32,
        )
        * scaled_gradient
    )
    up_weight_gradient = (
        ADAPTER_SCALE
        * lax.dot_general(
            rank_reduced,
            row_gradients.astype(jnp.float32),
            (((0,), (0,)), ((), ())),
            precision=highest,
            preferred_element_type=jnp.float32,
        )
        * scaled_gradient
    )
    back = lax.all_to_all(
        jnp.concatenate([spread, lifted], axis=1).reshape(groups, capacity, model_width + value_width),
        "agent",
        split_axis=0,
        concat_axis=0,
        tiled=True,
    ).reshape(slot_count, model_width + value_width)
    grad_down, up_weight_gradient = lax.psum((grad_down, up_weight_gradient), "dp")
    raised_rows = lax.dot_general(
        packing,
        back[:, model_width:],
        (((0,), (0,)), ((), ())),
        preferred_element_type=jnp.float32,
    )
    spread_rows = lax.dot_general(
        packing,
        back[:, :model_width],
        (((0,), (0,)), ((), ())),
        preferred_element_type=jnp.float32,
    )
    raised_rows, spread_rows, down_grad, up_grad = (
        raised_rows,
        spread_rows,
        grad_down[None],
        up_weight_gradient[None],
    )
    value_output = (value_projected + ADAPTER_SCALE * raised_rows).astype(jnp.bfloat16)
    input_grad = (backward + spread_rows).astype(jnp.bfloat16)
    return (value_output, input_grad, down_grad, up_grad)


def solution(mesh):
    return jax.shard_map(
        per_device,
        mesh=mesh,
        in_specs=(
            P(("dp", "agent"), None),
            P(("dp", "agent"), None),
            P(("dp", "agent"), None),
            P(("dp", "agent"), None),
            P("agent", None, None),
            P("agent", None, None),
        ),
        out_specs=(
            P(("dp", "agent"), None),
            P(("dp", "agent"), None),
            P("agent", None, None),
            P("agent", None, None),
        ),
        check_vma=False,
    )
```

```python
import math

import jax
import jax.numpy as jnp
from jax import lax
from jax.sharding import PartitionSpec as P

ADAPTER_SCALE = 2.0


def per_device(
    activations,
    row_agent_index,
    output_gradient,
    frozen_value_weight,
    adapter_down_weight,
    adapter_up_weight,
):
    groups = lax.axis_size("agent")
    tok_rows = activations.shape[0]
    model_width = activations.shape[1]
    value_width = output_gradient.shape[1]
    capacity = 2 * tok_rows // groups
    slot_count = groups * capacity
    scaled_gradient = 1.0 / math.sqrt(tok_rows * lax.axis_size("dp"))
    highest = lax.Precision.HIGHEST
    owner_ids = row_agent_index[:, 0]
    onehot = (owner_ids[:, None] == jnp.arange(groups, dtype=jnp.int32)[None, :]).astype(
        jnp.bfloat16
    )
    earlier = (jnp.arange(tok_rows)[None, :] < jnp.arange(tok_rows)[:, None]).astype(jnp.bfloat16)
    before = jnp.dot(earlier, onehot, preferred_element_type=jnp.float32)
    slot_rank = jnp.sum(before * onehot.astype(jnp.float32), axis=1).astype(jnp.int32)
    target = owner_ids * capacity + slot_rank
    packing = (jnp.arange(slot_count, dtype=jnp.int32)[:, None] == target[None, :]).astype(
        jnp.bfloat16
    )
    block_rows = frozen_value_weight.shape[0]
    padded = jnp.concatenate([frozen_value_weight, jnp.zeros_like(frozen_value_weight)], axis=0)
    plane_weight = lax.all_gather(padded, "agent", axis=0, tiled=False)[:, :block_rows]
    whole_weight = lax.all_gather(plane_weight, "dp", axis=0, tiled=False).reshape(
        -1, frozen_value_weight.shape[1]
    )
    value_projected = jnp.dot(activations, whole_weight, preferred_element_type=jnp.float32)
    backward = lax.dot_general(
        output_gradient, whole_weight, (((1,), (1,)), ((), ())), preferred_element_type=jnp.float32
    )
    value_projected, backward = (value_projected, backward)
    both = jnp.concatenate([activations, output_gradient], axis=1)
    send = jnp.dot(packing, both, preferred_element_type=jnp.float32).astype(jnp.bfloat16)
    recv = lax.all_to_all(
        send.reshape(groups, capacity, model_width + value_width),
        "agent",
        split_axis=0,
        concat_axis=0,
        tiled=True,
    ).reshape(slot_count, model_width + value_width)
    rows_x = recv[:, :model_width]
    row_gradients = recv[:, model_width:]
    down_weight = adapter_down_weight[0]
    up_weight = adapter_up_weight[0]
    down_wide = down_weight.astype(jnp.float32)
    up_wide = up_weight.astype(jnp.float32)
    rank_reduced = lax.dot_general(
        rows_x, down_weight, (((1,), (1,)), ((), ())), preferred_element_type=jnp.float32
    )
    lifted = jnp.dot(
        rank_reduced, up_wide, precision=highest, preferred_element_type=jnp.float32
    ).astype(jnp.bfloat16)
    collected_rows = ADAPTER_SCALE * lax.dot_general(
        row_gradients, up_weight, (((1,), (1,)), ((), ())), preferred_element_type=jnp.float32
    )
    spread = jnp.dot(
        collected_rows, down_wide, precision=highest, preferred_element_type=jnp.float32
    ).astype(jnp.bfloat16)
    grad_down = (
        lax.dot_general(
            collected_rows,
            rows_x.astype(jnp.float32),
            (((0,), (0,)), ((), ())),
            precision=highest,
            preferred_element_type=jnp.float32,
        )
        * scaled_gradient
    )
    up_weight_gradient = (
        ADAPTER_SCALE
        * lax.dot_general(
            rank_reduced,
            row_gradients.astype(jnp.float32),
            (((0,), (0,)), ((), ())),
            precision=highest,
            preferred_element_type=jnp.float32,
        )
        * scaled_gradient
    )
    back = lax.all_to_all(
        jnp.concatenate([spread, lifted], axis=1).reshape(groups, capacity, model_width + value_width),
        "agent",
        split_axis=0,
        concat_axis=0,
        tiled=True,
    ).reshape(slot_count, model_width + value_width)
    grad_down, up_weight_gradient = lax.psum((grad_down, up_weight_gradient), "dp")
    raised_rows = lax.dot_general(
        packing,
        back[:, model_width:],
        (((0,), (0,)), ((), ())),
        preferred_element_type=jnp.float32,
    )
    spread_rows = lax.dot_general(
        packing,
        back[:, :model_width],
        (((0,), (0,)), ((), ())),
        preferred_element_type=jnp.float32,
    )
    raised_rows, spread_rows, down_grad, up_grad = (
        raised_rows,
        spread_rows,
        grad_down[None],
        up_weight_gradient[None],
    )
    value_output = (value_projected + ADAPTER_SCALE * raised_rows).astype(jnp.bfloat16)
    input_grad = (backward + spread_rows).astype(jnp.bfloat16)
    return (value_output, input_grad, down_grad, up_grad)


def solution(mesh):
    return jax.shard_map(
        per_device,
        mesh=mesh,
        in_specs=(
            P(("dp", "agent"), None),
            P(("dp", "agent"), None),
            P(("dp", "agent"), None),
            P(("dp", "agent"), None),
            P("agent", None, None),
            P("agent", None, None),
        ),
        out_specs=(
            P(("dp", "agent"), None),
            P(("dp", "agent"), None),
            P("agent", None, None),
            P("agent", None, None),
        ),
        check_vma=False,
    )
```

```python
import math

import jax
import jax.numpy as jnp
from jax import lax
from jax.sharding import PartitionSpec as P


ADAPTER_SCALE = 2.0


def _dp_sum(grad_down, grad_up):
    parts = lax.axis_size("dp")
    total = (grad_down, grad_up)
    step = 1
    while step < parts:
        pairs = [(i, i ^ step) for i in range(parts)]
        theirs = lax.ppermute(total, "dp", pairs)
        total = (total[0] + theirs[0], total[1] + theirs[1])
        step *= 2
    return total


def _body(
    activations,
    row_agent_index,
    output_gradient,
    frozen_value_weight,
    adapter_down_weight,
    adapter_up_weight,
):
    groups = lax.axis_size("agent")
    tok_rows = activations.shape[0]
    model_width = activations.shape[1]
    value_width = output_gradient.shape[1]
    capacity = 2 * tok_rows // groups
    slot_count = groups * capacity
    scaled_gradient = 1.0 / math.sqrt(tok_rows * lax.axis_size("dp"))
    highest = lax.Precision.HIGHEST
    owner_ids = row_agent_index[:, 0]
    onehot = (owner_ids[:, None] == jnp.arange(groups, dtype=jnp.int32)[None, :]).astype(
        jnp.bfloat16
    )
    earlier = (jnp.arange(tok_rows)[None, :] < jnp.arange(tok_rows)[:, None]).astype(jnp.bfloat16)
    before = jnp.dot(earlier, onehot, preferred_element_type=jnp.float32)
    slot_rank = jnp.sum(before * onehot.astype(jnp.float32), axis=1).astype(jnp.int32)
    target = owner_ids * capacity + slot_rank
    packing = (jnp.arange(slot_count, dtype=jnp.int32)[:, None] == target[None, :]).astype(
        jnp.bfloat16
    )
    block_rows = frozen_value_weight.shape[0]
    padded = jnp.concatenate([frozen_value_weight, jnp.zeros_like(frozen_value_weight)], axis=0)
    plane_weight = lax.all_gather(padded, "agent", axis=0, tiled=False)[:, :block_rows]
    both = jnp.concatenate([activations, output_gradient], axis=1)
    send = jnp.dot(packing, both, preferred_element_type=jnp.float32).astype(jnp.bfloat16)
    recv = lax.all_to_all(
        send.reshape(groups, capacity, model_width + value_width),
        "agent",
        split_axis=0,
        concat_axis=0,
        tiled=True,
    ).reshape(slot_count, model_width + value_width)
    plane_weight, recv = lax.optimization_barrier((plane_weight, recv))
    whole_weight = lax.all_gather(plane_weight, "dp", axis=0, tiled=False).reshape(
        -1, frozen_value_weight.shape[1]
    )
    value_projected = jnp.dot(activations, whole_weight, preferred_element_type=jnp.float32)
    backward = lax.dot_general(
        output_gradient, whole_weight, (((1,), (1,)), ((), ())), preferred_element_type=jnp.float32
    )
    rows_x = recv[:, :model_width]
    row_gradients = recv[:, model_width:]
    down_weight = adapter_down_weight[0]
    up_weight = adapter_up_weight[0]
    down_wide = down_weight.astype(jnp.float32)
    up_wide = up_weight.astype(jnp.float32)
    rank_reduced = lax.dot_general(
        rows_x, down_weight, (((1,), (1,)), ((), ())), preferred_element_type=jnp.float32
    )
    lifted = jnp.dot(
        rank_reduced, up_wide, precision=highest, preferred_element_type=jnp.float32
    ).astype(jnp.bfloat16)
    collected_rows = ADAPTER_SCALE * lax.dot_general(
        row_gradients, up_weight, (((1,), (1,)), ((), ())), preferred_element_type=jnp.float32
    )
    spread = jnp.dot(
        collected_rows, down_wide, precision=highest, preferred_element_type=jnp.float32
    ).astype(jnp.bfloat16)
    grad_down = (
        lax.dot_general(
            collected_rows,
            rows_x.astype(jnp.float32),
            (((0,), (0,)), ((), ())),
            precision=highest,
            preferred_element_type=jnp.float32,
        )
        * scaled_gradient
    )
    up_weight_gradient = (
        ADAPTER_SCALE
        * lax.dot_general(
            rank_reduced,
            row_gradients.astype(jnp.float32),
            (((0,), (0,)), ((), ())),
            precision=highest,
            preferred_element_type=jnp.float32,
        )
        * scaled_gradient
    )
    back = lax.all_to_all(
        jnp.concatenate([spread, lifted], axis=1).reshape(groups, capacity, model_width + value_width),
        "agent",
        split_axis=0,
        concat_axis=0,
        tiled=True,
    ).reshape(slot_count, model_width + value_width)
    grad_down, up_weight_gradient = _dp_sum(grad_down, up_weight_gradient)
    raised_rows = lax.dot_general(
        packing,
        back[:, model_width:],
        (((0,), (0,)), ((), ())),
        preferred_element_type=jnp.float32,
    )
    spread_rows = lax.dot_general(
        packing,
        back[:, :model_width],
        (((0,), (0,)), ((), ())),
        preferred_element_type=jnp.float32,
    )
    raised_rows, spread_rows, down_grad, up_grad = (
        raised_rows,
        spread_rows,
        grad_down[None],
        up_weight_gradient[None],
    )
    value_output = (value_projected + ADAPTER_SCALE * raised_rows).astype(jnp.bfloat16)
    input_grad = (backward + spread_rows).astype(jnp.bfloat16)
    return (value_output, input_grad, down_grad, up_grad)


def solution(mesh):
    return jax.shard_map(
        _body,
        mesh=mesh,
        in_specs=(
            P(("dp", "agent"), None),
            P(("dp", "agent"), None),
            P(("dp", "agent"), None),
            P(("dp", "agent"), None),
            P("agent", None, None),
            P("agent", None, None),
        ),
        out_specs=(
            P(("dp", "agent"), None),
            P(("dp", "agent"), None),
            P("agent", None, None),
            P("agent", None, None),
        ),
        check_vma=False,
    )
```

```python
import math

import jax
import jax.numpy as jnp
from jax import lax
from jax.sharding import PartitionSpec as P

ADAPTER_SCALE = 2.0


def per_device(
    activations,
    row_agent_index,
    output_gradient,
    frozen_value_weight,
    adapter_down_weight,
    adapter_up_weight,
):
    groups = lax.axis_size("agent")
    tok_rows = activations.shape[0]
    model_width = activations.shape[1]
    value_width = output_gradient.shape[1]
    capacity = 2 * tok_rows // groups
    slot_count = groups * capacity
    scaled_gradient = 1.0 / math.sqrt(tok_rows * lax.axis_size("dp"))
    highest = lax.Precision.HIGHEST
    owner_ids = row_agent_index[:, 0]
    onehot = (owner_ids[:, None] == jnp.arange(groups, dtype=jnp.int32)[None, :]).astype(
        jnp.bfloat16
    )
    earlier = (jnp.arange(tok_rows)[None, :] < jnp.arange(tok_rows)[:, None]).astype(jnp.bfloat16)
    before = jnp.dot(earlier, onehot, preferred_element_type=jnp.float32)
    slot_rank = jnp.sum(before * onehot.astype(jnp.float32), axis=1).astype(jnp.int32)
    target = owner_ids * capacity + slot_rank
    packing = (jnp.arange(slot_count, dtype=jnp.int32)[:, None] == target[None, :]).astype(
        jnp.bfloat16
    )
    whole_weight = lax.all_gather(frozen_value_weight, ("dp", "agent"), axis=0, tiled=True)
    value_projected = jnp.dot(activations, whole_weight, preferred_element_type=jnp.float32)
    backward = lax.dot_general(
        output_gradient, whole_weight, (((1,), (1,)), ((), ())), preferred_element_type=jnp.float32
    )
    value_projected, backward = lax.optimization_barrier((value_projected, backward))
    both = jnp.concatenate([activations, output_gradient], axis=1)
    send = jnp.dot(packing, both, preferred_element_type=jnp.float32).astype(jnp.bfloat16)
    recv = lax.all_to_all(
        send.reshape(groups, capacity, model_width + value_width),
        "agent",
        split_axis=0,
        concat_axis=0,
        tiled=True,
    ).reshape(slot_count, model_width + value_width)
    rows_x = recv[:, :model_width]
    row_gradients = recv[:, model_width:]
    down_weight = adapter_down_weight[0]
    up_weight = adapter_up_weight[0]
    down_wide = down_weight.astype(jnp.float32)
    up_wide = up_weight.astype(jnp.float32)
    rank_reduced = lax.dot_general(
        rows_x, down_weight, (((1,), (1,)), ((), ())), preferred_element_type=jnp.float32
    )
    lifted = jnp.dot(
        rank_reduced, up_wide, precision=highest, preferred_element_type=jnp.float32
    ).astype(jnp.bfloat16)
    collected_rows = ADAPTER_SCALE * lax.dot_general(
        row_gradients, up_weight, (((1,), (1,)), ((), ())), preferred_element_type=jnp.float32
    )
    spread = jnp.dot(
        collected_rows, down_wide, precision=highest, preferred_element_type=jnp.float32
    ).astype(jnp.bfloat16)
    grad_down = (
        lax.dot_general(
            collected_rows,
            rows_x.astype(jnp.float32),
            (((0,), (0,)), ((), ())),
            precision=highest,
            preferred_element_type=jnp.float32,
        )
        * scaled_gradient
    )
    up_weight_gradient = (
        ADAPTER_SCALE
        * lax.dot_general(
            rank_reduced,
            row_gradients.astype(jnp.float32),
            (((0,), (0,)), ((), ())),
            precision=highest,
            preferred_element_type=jnp.float32,
        )
        * scaled_gradient
    )
    back = lax.all_to_all(
        jnp.concatenate([spread, lifted], axis=1).reshape(groups, capacity, model_width + value_width),
        "agent",
        split_axis=0,
        concat_axis=0,
        tiled=True,
    ).reshape(slot_count, model_width + value_width)
    grad_down, up_weight_gradient = lax.psum((grad_down, up_weight_gradient), "dp")
    raised_rows = lax.dot_general(
        packing,
        back[:, model_width:],
        (((0,), (0,)), ((), ())),
        preferred_element_type=jnp.float32,
    )
    spread_rows = lax.dot_general(
        packing,
        back[:, :model_width],
        (((0,), (0,)), ((), ())),
        preferred_element_type=jnp.float32,
    )
    raised_rows, spread_rows, down_grad, up_grad = (
        raised_rows,
        spread_rows,
        grad_down[None],
        up_weight_gradient[None],
    )
    value_output = (value_projected + ADAPTER_SCALE * raised_rows).astype(jnp.bfloat16)
    input_grad = (backward + spread_rows).astype(jnp.bfloat16)
    return (value_output, input_grad, down_grad, up_grad)


def solution(mesh):
    return jax.shard_map(
        per_device,
        mesh=mesh,
        in_specs=(
            P(("dp", "agent"), None),
            P(("dp", "agent"), None),
            P(("dp", "agent"), None),
            P(("dp", "agent"), None),
            P("agent", None, None),
            P("agent", None, None),
        ),
        out_specs=(
            P(("dp", "agent"), None),
            P(("dp", "agent"), None),
            P("agent", None, None),
            P("agent", None, None),
        ),
        check_vma=False,
    )
```

```python
import math

import jax
import jax.numpy as jnp
from jax import lax
from jax.sharding import PartitionSpec as P

ADAPTER_SCALE = 2.0


def per_device(
    activations,
    row_agent_index,
    output_gradient,
    frozen_value_weight,
    adapter_down_weight,
    adapter_up_weight,
):
    groups = lax.axis_size("agent")
    tok_rows = activations.shape[0]
    model_width = activations.shape[1]
    value_width = output_gradient.shape[1]
    capacity = 2 * tok_rows // groups
    slot_count = groups * capacity
    scaled_gradient = 1.0 / math.sqrt(tok_rows * lax.axis_size("dp"))
    highest = lax.Precision.HIGHEST
    owner_ids = row_agent_index[:, 0]
    onehot = (owner_ids[:, None] == jnp.arange(groups, dtype=jnp.int32)[None, :]).astype(
        jnp.bfloat16
    )
    earlier = (jnp.arange(tok_rows)[None, :] < jnp.arange(tok_rows)[:, None]).astype(jnp.bfloat16)
    before = jnp.dot(earlier, onehot, preferred_element_type=jnp.float32)
    slot_rank = jnp.sum(before * onehot.astype(jnp.float32), axis=1).astype(jnp.int32)
    target = owner_ids * capacity + slot_rank
    packing = (jnp.arange(slot_count, dtype=jnp.int32)[:, None] == target[None, :]).astype(
        jnp.bfloat16
    )
    dp_size = lax.axis_size("dp")
    block = frozen_value_weight.shape[0]
    whole_weight = lax.all_gather(frozen_value_weight, ("agent", "dp"), axis=0, tiled=True)
    turned_x = (
        activations.reshape(tok_rows, dp_size, groups, block)
        .transpose(0, 2, 1, 3)
        .reshape(tok_rows, model_width)
    )
    value_projected = jnp.dot(turned_x, whole_weight, preferred_element_type=jnp.float32)
    turned_back = lax.dot_general(
        output_gradient, whole_weight, (((1,), (1,)), ((), ())), preferred_element_type=jnp.float32
    )
    backward = (
        turned_back.reshape(tok_rows, groups, dp_size, block)
        .transpose(0, 2, 1, 3)
        .reshape(tok_rows, model_width)
    )
    value_projected, backward = lax.optimization_barrier((value_projected, backward))
    both = jnp.concatenate([activations, output_gradient], axis=1)
    send = jnp.dot(packing, both, preferred_element_type=jnp.float32).astype(jnp.bfloat16)
    recv = lax.all_to_all(
        send.reshape(groups, capacity, model_width + value_width),
        "agent",
        split_axis=0,
        concat_axis=0,
        tiled=True,
    ).reshape(slot_count, model_width + value_width)
    rows_x = recv[:, :model_width]
    row_gradients = recv[:, model_width:]
    down_weight = adapter_down_weight[0]
    up_weight = adapter_up_weight[0]
    down_wide = down_weight.astype(jnp.float32)
    up_wide = up_weight.astype(jnp.float32)
    rank_reduced = lax.dot_general(
        rows_x, down_weight, (((1,), (1,)), ((), ())), preferred_element_type=jnp.float32
    )
    lifted = jnp.dot(
        rank_reduced, up_wide, precision=highest, preferred_element_type=jnp.float32
    ).astype(jnp.bfloat16)
    collected_rows = ADAPTER_SCALE * lax.dot_general(
        row_gradients, up_weight, (((1,), (1,)), ((), ())), preferred_element_type=jnp.float32
    )
    spread = jnp.dot(
        collected_rows, down_wide, precision=highest, preferred_element_type=jnp.float32
    ).astype(jnp.bfloat16)
    grad_down = (
        lax.dot_general(
            collected_rows,
            rows_x.astype(jnp.float32),
            (((0,), (0,)), ((), ())),
            precision=highest,
            preferred_element_type=jnp.float32,
        )
        * scaled_gradient
    )
    up_weight_gradient = (
        ADAPTER_SCALE
        * lax.dot_general(
            rank_reduced,
            row_gradients.astype(jnp.float32),
            (((0,), (0,)), ((), ())),
            precision=highest,
            preferred_element_type=jnp.float32,
        )
        * scaled_gradient
    )
    back = lax.all_to_all(
        jnp.concatenate([spread, lifted], axis=1).reshape(groups, capacity, model_width + value_width),
        "agent",
        split_axis=0,
        concat_axis=0,
        tiled=True,
    ).reshape(slot_count, model_width + value_width)
    grad_down, up_weight_gradient = lax.psum((grad_down, up_weight_gradient), "dp")
    raised_rows = lax.dot_general(
        packing,
        back[:, model_width:],
        (((0,), (0,)), ((), ())),
        preferred_element_type=jnp.float32,
    )
    spread_rows = lax.dot_general(
        packing,
        back[:, :model_width],
        (((0,), (0,)), ((), ())),
        preferred_element_type=jnp.float32,
    )
    raised_rows, spread_rows, down_grad, up_grad = (
        raised_rows,
        spread_rows,
        grad_down[None],
        up_weight_gradient[None],
    )
    value_output = (value_projected + ADAPTER_SCALE * raised_rows).astype(jnp.bfloat16)
    input_grad = (backward + spread_rows).astype(jnp.bfloat16)
    return (value_output, input_grad, down_grad, up_grad)


def solution(mesh):
    return jax.shard_map(
        per_device,
        mesh=mesh,
        in_specs=(
            P(("dp", "agent"), None),
            P(("dp", "agent"), None),
            P(("dp", "agent"), None),
            P(("dp", "agent"), None),
            P("agent", None, None),
            P("agent", None, None),
        ),
        out_specs=(
            P(("dp", "agent"), None),
            P(("dp", "agent"), None),
            P("agent", None, None),
            P("agent", None, None),
        ),
        check_vma=False,
    )
```
